512 devices in a mesh: grp: 8 (over z_hi, core), req: 64 (over y, x, z_lo).
Axes of the slice: x: 4, y: 8, z: 8 (z_hi: 4, z_lo: 2; z = z_hi * 2 + z_lo), core: 2. Of those that a mesh axis runs over, the one named last changes fastest.
Arguments:
- queries: bfloat16 [8, 64, 4, 2048], P('grp', 'req'), may hold values from -12 to 1700
- suffix_kv: bfloat16 [8, 64, 2, 4, 512], P('grp', 'req'), may hold values from -6 to 6
- prefix_pool: bfloat16 [8, 64, 3, 2, 128, 512], P('grp', 'req'), may hold values from -6 to 6
- page_table: int32 [64, 16], P('req'), may hold values from 0 to 23, as said below
- suffix_len: int32 [8, 64], P('grp'), may hold values from 1 to 4, 128 in all within a row
- residual: bfloat16 [8, 256, 4096], P('grp', None, 'req'), may hold values from -40 to 40
- out_weight: bfloat16 [2048, 4096], P(None, 'req'), may hold values from -0.5 to 0.5
- norm_gain: bfloat16 [4096], P('req'), may hold values from 0.099609375 to 1.8984375
- gate_up: bfloat16 [2, 4096, 8192], P(None, None, 'req'), may hold values from -0.09375 to 0.09375
- down_weight: bfloat16 [8192, 4096], P('req'), may hold values from -0.1875 to 0.1875
Outputs:
- hidden_out: bfloat16 [8, 256, 4096], P('grp', None, 'req')
The draws below stay inside these ranges and needn't reach their ends.
Inputs may be any that keep to these rules, and one draw needn't show every extreme that they name: `page_table`: row b lists 16 different pages of group b's pool; pool page p is slot p % 3 on the member p // 3.
All inputs are finite; a program needn't handle non-finite values.
Results may differ from the reference program's by a relative error of at most 0.028.
Values may be sent and summed in bfloat16 or wider, within the bound.
No kernel may reach another device: no remote copies, remote signals or barrier semaphores. Data moves between devices by JAX's collectives and lax.ppermute only.
A program may use at most 64 MiB of HBM per device.

```python
import math
import jax
import jax.numpy as jnp
import numpy as np
from jax import lax

D = 4096
HD = 128
QH = 16
KVH = 4
FF = 8192
PAGE = 128
POOL_DEV = 3
SLOTS = 4
PAGES = 16
QW = 2048
KW = 512
N_GRP = 8
N_REQ = 64


def draw_queries(key, part):
    array_shape = (N_GRP, N_REQ, SLOTS, QH * HD)
    values_drawn = jnp.clip(2.0 * jax.random.normal(key, array_shape, jnp.float32), -12.0, 12.0)
    return values_drawn.astype(jnp.bfloat16)


def draw_prefix_pool(key, part):
    array_shape = (N_GRP, N_REQ, POOL_DEV, 2, PAGE, KVH * HD)
    values_drawn = jnp.clip(jax.random.normal(key, array_shape, jnp.float32), -6.0, 6.0)
    return values_drawn.astype(jnp.bfloat16)


def draw_page_table(key, part):
    pool_size = N_GRP * POOL_DEV

    def one_row(row_index):
        shuffled = jax.random.permutation(jax.random.fold_in(key, row_index), pool_size)
        return shuffled[:PAGES].astype(jnp.int32)
    table_rows = jax.vmap(one_row)(jnp.arange(N_REQ, dtype=jnp.int32))
    middle_pages = jax.random.permutation(jax.random.fold_in(key, 1000003), pool_size - 2) + 1
    first_row = jnp.concatenate([jnp.array([0, pool_size - 1], jnp.int32), middle_pages[:PAGES - 2].astype(jnp.int32)])
    return table_rows.at[0].set(first_row)


def draw_residual(key, part):
    array_shape = (N_GRP, N_REQ * SLOTS, D)
    column_scale = jnp.exp(jnp.log(3.0) * jnp.arange(D, dtype=jnp.float32) / D)
    values_drawn = jnp.clip(jax.random.normal(key, array_shape, jnp.float32), -6.0, 6.0) * column_scale * 0.6
    return values_drawn.astype(jnp.bfloat16)


def spiked(drawn, stream_key, source, target, parts, factor):
    owner, partner = [(jnp.arange(drawn.shape[axis_at]) // (drawn.shape[axis_at] // parts)).reshape([-1 if axis == axis_at else 1 for axis in range(drawn.ndim)]) for axis_at in (source, target)]
    chosen = jax.random.permutation(stream_key, parts)[partner]
    strong = (owner == chosen) | (owner == (partner + parts // 2) % parts)
    return jnp.where(strong, factor * drawn, drawn)


def shard_levels(key, dims, shards, low, top_value):
    factor_of, own = 1.0, jax.random.fold_in(key, 6)
    for position, blocks in shards:
        steps = jnp.exp(jax.random.uniform(jax.random.fold_in(own, position), (blocks,), jnp.float32, low / len(shards), top_value / len(shards)))
        factor_of = factor_of * jnp.repeat(steps, dims[position] // blocks).reshape([-1 if axis == position else 1 for axis in range(len(dims))])
    return factor_of


def length_profile(amount, total, bound, lean):
    portions = [(1 << 20) // math.isqrt(rank ** lean) + 1 for rank in range(2, amount + 1)]
    spare, counts = total - bound - (amount - 1), [1] * (amount - 1)
    while spare > 0:
        free = [i for i in range(amount - 1) if counts[i] < bound]
        mass, remaining = sum([portions[i] for i in free]), spare
        for i in free:
            extra = min(bound - counts[i], max(1, remaining * portions[i] // mass), spare)
            counts[i] = counts[i] + extra
            spare = spare - extra
    return np.array([bound] + counts)


def ragged_sizes(stream_key, count, total, reach, lean):
    if count == 2:
        one = jax.random.randint(stream_key, (), max(1, total - reach), min(reach, total - 1) + 1)
        return jnp.stack([one, total - one])
    sizes = jnp.asarray(length_profile(count, total, reach, lean), jnp.int32)
    couples = (count - 1) // 2
    giver, receiver = sizes[1:1 + 2 * couples:2], sizes[2:2 + 2 * couples:2]
    room = jnp.minimum(giver - 1, reach - receiver)
    passed = jax.random.randint(jax.random.fold_in(stream_key, 1), (couples,), 0, 1 << 20) % (room + 1)
    sizes = sizes.at[1:1 + 2 * couples:2].set(giver - passed).at[2:2 + 2 * couples:2].set(receiver + passed)
    return sizes[jax.random.permutation(jax.random.fold_in(stream_key, 2), count)]


def scatter_about(rng, dims, scale, bound, shards=(), kind=jnp.bfloat16):
    drawn = scale * jax.random.normal(rng, dims, jnp.float32)
    if shards:
        drawn = drawn * shard_levels(rng, dims, shards, -0.22, 0.18)
    return jnp.clip(drawn, -bound, bound).astype(kind)


def heavy_noise(key, extent, scale, limit, shards, heavy, kind=jnp.bfloat16):
    result = scale * jax.random.normal(key, extent, jnp.float32)
    if shards:
        result = result * shard_levels(key, extent, shards, -0.22, 0.18)
    return jnp.clip(spiked(result, jax.random.fold_in(key, 3), *heavy), -limit, limit).astype(kind)


def setup_inputs(seed: int = 0) -> dict:
    streams_of = jax.random.split(jax.random.key(seed), 11)
    return {
        "queries": draw_queries(jax.random.fold_in(streams_of[10], 71), 0),
        "suffix_kv": scatter_about(streams_of[1], (N_GRP, N_REQ, 2, SLOTS, KW), 1.0, 6.0, ((0, 8), (1, 64))),
        "prefix_pool": draw_prefix_pool(jax.random.fold_in(streams_of[10], 71), 0),
        "page_table": draw_page_table(jax.random.fold_in(streams_of[10], 71), 0),
        "suffix_len": jax.vmap(lambda own: ragged_sizes(own, N_REQ, N_REQ * SLOTS // 2, SLOTS, 2))(jax.random.split(streams_of[4], N_GRP)).reshape((N_GRP, N_REQ)).astype(jnp.int32),
        "residual": draw_residual(jax.random.fold_in(streams_of[10], 71), 0),
        "out_weight": scatter_about(streams_of[6], (QW, D), (QW // 16) ** -0.5, 0.5, ((1, 64),)),
        "norm_gain": jnp.clip(1.0 + 0.18 * jax.random.normal(streams_of[7], (D,), jnp.float32), 0.099609375, 1.8984375).astype(jnp.bfloat16),
        "gate_up": scatter_about(streams_of[8], (2, D, FF), D ** -0.5, 0.09375, ((2, 64),)),
        "down_weight": heavy_noise(streams_of[9], (FF, D), FF ** -0.5, 0.1875, ((0, 64),), (0, 1, 64, 4.0)),
    }


def attend_group(group_block):
    group_queries, group_suffix, group_pool, table_row = group_block
    group_size = QH // KVH
    pool_flat = group_pool.reshape(N_GRP * POOL_DEV, 2, PAGE, KVH * HD)
    chosen_pages = jnp.take(pool_flat, table_row.astype(jnp.int32), axis=0)
    prefix_keys = chosen_pages[:, 0].reshape(PAGES * PAGE, KVH, HD).astype(jnp.float32)
    prefix_values = chosen_pages[:, 1].reshape(PAGES * PAGE, KVH, HD).astype(jnp.float32)
    query_heads = group_queries.astype(jnp.float32).reshape(N_GRP, SLOTS, KVH, group_size, HD)
    own_keys = group_suffix[:, 0].astype(jnp.float32).reshape(N_GRP, SLOTS, KVH, HD)
    own_values = group_suffix[:, 1].astype(jnp.float32).reshape(N_GRP, SLOTS, KVH, HD)
    prefix_scores = jnp.einsum('asjgd,tjd->ajgst', query_heads, prefix_keys) * HD ** (-0.5)
    suffix_scores = jnp.einsum('asjgd,atjd->ajgst', query_heads, own_keys) * HD ** (-0.5)
    causal = jnp.arange(SLOTS)[:, None] >= jnp.arange(SLOTS)[None, :]
    suffix_scores = jnp.where(causal, suffix_scores, -jnp.inf)
    running_max = jnp.maximum(lax.optimization_barrier(jnp.max(prefix_scores, axis=-1)), lax.optimization_barrier(jnp.max(suffix_scores, axis=-1)))
    prefix_weights = jnp.exp(prefix_scores - running_max[..., None])
    suffix_weights = jnp.exp(suffix_scores - running_max[..., None])
    weight_sum = lax.optimization_barrier(jnp.sum(prefix_weights, axis=-1)) + lax.optimization_barrier(jnp.sum(suffix_weights, axis=-1))
    prefix_rounded = lax.optimization_barrier(prefix_weights.astype(jnp.bfloat16)).astype(jnp.float32)
    suffix_rounded = lax.optimization_barrier(suffix_weights.astype(jnp.bfloat16)).astype(jnp.float32)
    accumulated = jnp.einsum('ajgst,tjd->ajgsd', prefix_rounded, prefix_values)
    accumulated = accumulated + jnp.einsum('ajgst,atjd->ajgsd', suffix_rounded, own_values)
    accumulated = accumulated / weight_sum[..., None]
    ordered = jnp.transpose(accumulated, (0, 3, 1, 2, 4))
    return ordered.reshape(N_GRP, SLOTS, QH * HD).astype(jnp.bfloat16)

def reference(queries, suffix_kv, prefix_pool, page_table, suffix_len, residual, out_weight, norm_gain, gate_up, down_weight):
    per_group = lax.map(attend_group, (jnp.moveaxis(queries, 1, 0), jnp.moveaxis(suffix_kv, 1, 0), jnp.moveaxis(prefix_pool, 1, 0), page_table))
    head_out = jnp.transpose(per_group, (1, 0, 2, 3)).reshape(N_GRP * N_REQ * SLOTS, QH * HD)
    projected = jnp.dot(head_out, out_weight, preferred_element_type=jnp.float32)
    flat_residual = residual.reshape(N_GRP * N_REQ * SLOTS, D).astype(jnp.float32)
    stream = (flat_residual + projected).astype(jnp.bfloat16)
    wide = stream.astype(jnp.float32)
    inverse_rms = lax.rsqrt(lax.optimization_barrier(jnp.mean(wide * wide, axis=1)) + 1e-05)
    normed = (wide * inverse_rms[:, None] * norm_gain.astype(jnp.float32)[None, :]).astype(jnp.bfloat16)
    gate = jnp.dot(normed, gate_up[0], preferred_element_type=jnp.float32)
    up_part = jnp.dot(normed, gate_up[1], preferred_element_type=jnp.float32)
    hidden = (jax.nn.silu(gate) * up_part).astype(jnp.bfloat16)
    down_part = jnp.dot(hidden, down_weight, preferred_element_type=jnp.float32)
    slot_index = jnp.arange(N_REQ * SLOTS, dtype=jnp.int32) % SLOTS
    slot_live = slot_index[None, :] < jnp.repeat(suffix_len, SLOTS, axis=1)
    live_flat = slot_live.reshape(N_GRP * N_REQ * SLOTS).astype(jnp.float32)
    result_rows = (wide + down_part) * live_flat[:, None]
    return result_rows.astype(jnp.bfloat16).reshape(N_GRP, N_REQ * SLOTS, D)
```

```python
import jax
import jax.numpy as jnp
from jax import lax
from jax.sharding import PartitionSpec as P

D = 4096
HD = 128
QH = 16
KVH = 4
PAGE = 128


def split_heads(query_rows):
    row_count = query_rows.shape[0]
    query_heads = query_rows.reshape(row_count, KVH, QH // KVH, HD)
    return jnp.transpose(query_heads, (1, 2, 0, 3))


def empty_state(row_count):
    running_max = jnp.full((KVH, QH // KVH, row_count), -1e30, jnp.float32)
    weight_sum = jnp.zeros((KVH, QH // KVH, row_count), jnp.float32)
    accumulated = jnp.zeros((KVH, QH // KVH, row_count, HD), jnp.float32)
    return (running_max, weight_sum, accumulated)


def page_block(softmax_state, pages_part, query_heads, table_row):
    running_max, weight_sum, accumulated = softmax_state
    page_count = pages_part.shape[0]
    page_index = jnp.arange(page_count, dtype=jnp.int32)
    page_used = jnp.any(page_index[:, None] == table_row[None, :], axis=1)
    token_live = jnp.repeat(page_used, PAGE)
    key_rows = pages_part[:, 0].reshape(page_count * PAGE, KVH, HD)
    value_rows = pages_part[:, 1].reshape(page_count * PAGE, KVH, HD)
    scores = jnp.einsum(
        "jgsd,tjd->jgst", query_heads, key_rows, preferred_element_type=jnp.float32
    ) * HD ** (-0.5)
    scores = jnp.where(token_live, scores, -1e30)
    merged_max = jnp.maximum(running_max, jnp.max(scores, axis=-1))
    weights = jnp.where(token_live, jnp.exp(scores - merged_max[..., None]), 0.0)
    weight_sum = jnp.sum(weights, axis=-1)
    weighted = jnp.einsum(
        "jgst,tjd->jgsd",
        weights.astype(jnp.bfloat16),
        value_rows,
        preferred_element_type=jnp.float32,
    )
    accumulated = weighted
    return (merged_max, weight_sum, accumulated)


def with_suffix(softmax_state, query_heads, own_suffix):
    running_max, weight_sum, accumulated = softmax_state
    row_count = query_heads.shape[2]
    key_rows = own_suffix[0].reshape(row_count, KVH, HD)
    value_rows = own_suffix[1].reshape(row_count, KVH, HD)
    scores = jnp.einsum(
        "jgsd,tjd->jgst", query_heads, key_rows, preferred_element_type=jnp.float32
    ) * HD ** (-0.5)
    causal = jnp.arange(row_count)[:, None] >= jnp.arange(row_count)[None, :]
    scores = jnp.where(causal, scores, -1e30)
    merged_max = jnp.maximum(running_max, jnp.max(scores, axis=-1))
    weights = jnp.where(causal, jnp.exp(scores - merged_max[..., None]), 0.0)
    rescale = jnp.exp(running_max - merged_max)
    weight_sum = weight_sum * rescale + jnp.sum(weights, axis=-1)
    weighted = jnp.einsum(
        "jgst,tjd->jgsd",
        weights.astype(jnp.bfloat16),
        value_rows,
        preferred_element_type=jnp.float32,
    )
    accumulated = accumulated * rescale[..., None] + weighted
    accumulated = accumulated / weight_sum[..., None]
    ordered = jnp.transpose(accumulated, (2, 0, 1, 3))
    return ordered.reshape(row_count, QH * HD).astype(jnp.bfloat16)


def gather_rows(block, count):
    spread = jnp.broadcast_to(block[None], (count,) + block.shape)
    return lax.all_to_all(spread, "req", 0, 0, tiled=False)


def body(
    queries,
    suffix_kv,
    prefix_pool,
    page_table,
    suffix_len,
    residual,
    out_weight,
    norm_gain,
    gate_up,
    down_weight,
):
    slot_count = queries.shape[2]
    own_queries = queries[0, 0]
    own_pool = prefix_pool[0, 0]
    table_row = page_table[0]
    own_heads = split_heads(own_queries)
    softmax_state = page_block(
        empty_state(slot_count),
        lax.all_gather(own_pool, "grp", axis=0, tiled=True),
        own_heads,
        table_row,
    )
    attention = with_suffix(softmax_state, own_heads, suffix_kv[0, 0])
    req_count = lax.psum(1, "req")
    projected = jnp.dot(
        gather_rows(attention, req_count).reshape(-1, attention.shape[-1]),
        out_weight,
        preferred_element_type=jnp.float32,
    )
    stream = (residual[0].astype(jnp.float32) + projected).astype(jnp.bfloat16)
    wide_local = stream.astype(jnp.float32)
    token_count, local_width = stream.shape
    with_gain = jnp.concatenate([stream, norm_gain.reshape(1, local_width)], axis=0)
    gathered = gather_rows(with_gain, req_count)
    full_stream = jnp.transpose(gathered[:, :token_count], (1, 0, 2)).reshape(token_count, -1)
    full_gain = gathered[:, token_count].reshape(-1)
    wide = full_stream.astype(jnp.float32)
    row_sumsq = jnp.sum(wide * wide, axis=1)
    inverse_rms = lax.rsqrt(row_sumsq / D + 1e-05)
    normed = (wide * inverse_rms[:, None] * full_gain.astype(jnp.float32)[None, :]).astype(
        jnp.bfloat16
    )
    gate_up_out = jnp.einsum(
        "nc,kcf->knf",
        normed,
        gate_up,
        preferred_element_type=jnp.float32,
    )
    hidden = (jax.nn.silu(gate_up_out[0]) * gate_up_out[1]).astype(jnp.bfloat16)
    partial_value = jnp.dot(hidden, down_weight, preferred_element_type=jnp.float32)
    blocks = jnp.transpose(
        partial_value.reshape(token_count, req_count, local_width), (1, 0, 2)
    )
    summed = jnp.sum(lax.all_to_all(blocks, "req", 0, 0, tiled=False), axis=0)
    lengths = suffix_len[0]
    slot_index = jnp.arange(stream.shape[0], dtype=jnp.int32) % slot_count
    slot_live = (slot_index < jnp.repeat(lengths, slot_count)).astype(jnp.float32)
    result_rows = (wide_local + summed) * slot_live[:, None]
    return result_rows.astype(jnp.bfloat16)[None]


def solution(mesh):
    return jax.shard_map(
        body,
        mesh=mesh,
        in_specs=(
            P("grp", "req", None, None),
            P("grp", "req", None, None, None),
            P("grp", "req", None, None, None, None),
            P("req", None),
            P("grp", None),
            P("grp", None, "req"),
            P(None, "req"),
            P("req"),
            P(None, None, "req"),
            P("req", None),
        ),
        out_specs=P("grp", None, "req"),
        check_vma=False,
    )
```

```python
import jax
import jax.numpy as jnp
from jax import lax
from jax.sharding import PartitionSpec as P

D = 4096
HD = 128
QH = 16
KVH = 4
PAGE = 128


def heads_of(rows):
    row_count = rows.shape[0]
    return jnp.transpose(rows.reshape(row_count, KVH, QH // KVH, HD), (1, 2, 0, 3))


def attend(own_queries, own_suffix, own_pool, table_row):
    slot_count = own_queries.shape[0]
    member_count = lax.psum(1, "grp")
    member = lax.axis_index("grp")
    pool_pages = own_pool.shape[0]
    spread = jnp.broadcast_to(own_queries[None], (member_count,) + own_queries.shape)
    all_queries = lax.all_to_all(spread, "grp", 0, 0, tiled=False)
    query_heads = heads_of(all_queries.reshape(member_count * slot_count, -1))
    page_ids = member * pool_pages + jnp.arange(pool_pages, dtype=jnp.int32)
    page_used = jnp.any(page_ids[:, None] == table_row[None, :], axis=1)
    token_live = jnp.repeat(page_used, PAGE)
    key_rows = own_pool[:, 0].reshape(pool_pages * PAGE, KVH, HD)
    value_rows = own_pool[:, 1].reshape(pool_pages * PAGE, KVH, HD)
    scores = jnp.einsum(
        "jgsd,tjd->jgst", query_heads, key_rows, preferred_element_type=jnp.float32
    ) * HD ** (-0.5)
    scores = jnp.where(token_live, scores, -1e30)
    local_max = jnp.max(scores, axis=-1)
    weights = jnp.where(token_live, jnp.exp(scores - local_max[..., None]), 0.0)
    local_sum = jnp.sum(weights, axis=-1)
    weighted = jnp.einsum(
        "jgst,tjd->jgsd",
        weights.astype(jnp.bfloat16),
        value_rows,
        preferred_element_type=jnp.float32,
    )
    packed = jnp.concatenate([weighted, local_max[..., None], local_sum[..., None]], axis=-1)
    packed = packed.reshape(KVH, QH // KVH, member_count, slot_count, HD + 2)
    packed = jnp.transpose(packed, (2, 0, 1, 3, 4))
    parts = lax.all_to_all(packed, "grp", 0, 0, tiled=False)
    part_acc = parts[..., :HD]
    part_max = parts[..., HD]
    part_sum = parts[..., HD + 1]
    own_heads = heads_of(own_queries)
    suffix_keys = own_suffix[0].reshape(slot_count, KVH, HD)
    suffix_values = own_suffix[1].reshape(slot_count, KVH, HD)
    suffix_scores = jnp.einsum(
        "jgsd,tjd->jgst", own_heads, suffix_keys, preferred_element_type=jnp.float32
    ) * HD ** (-0.5)
    causal = jnp.arange(slot_count)[:, None] >= jnp.arange(slot_count)[None, :]
    suffix_scores = jnp.where(causal, suffix_scores, -1e30)
    merged_max = jnp.maximum(jnp.max(part_max, axis=0), jnp.max(suffix_scores, axis=-1))
    rescale = jnp.exp(part_max - merged_max[None])
    suffix_weights = jnp.where(causal, jnp.exp(suffix_scores - merged_max[..., None]), 0.0)
    total = jnp.sum(part_sum * rescale, axis=0) + jnp.sum(suffix_weights, axis=-1)
    accumulated = jnp.sum(part_acc * rescale[..., None], axis=0) + jnp.einsum(
        "jgst,tjd->jgsd",
        suffix_weights.astype(jnp.bfloat16),
        suffix_values,
        preferred_element_type=jnp.float32,
    )
    accumulated = accumulated / total[..., None]
    ordered = jnp.transpose(accumulated, (2, 0, 1, 3))
    return ordered.reshape(slot_count, QH * HD).astype(jnp.bfloat16)


def gather_rows(block, count):
    spread = jnp.broadcast_to(block[None], (count,) + block.shape)
    return lax.all_to_all(spread, "req", 0, 0, tiled=False)


def body(
    queries,
    suffix_kv,
    prefix_pool,
    page_table,
    suffix_len,
    residual,
    out_weight,
    norm_gain,
    gate_up,
    down_weight,
):
    slot_count = queries.shape[2]
    attention = attend(queries[0, 0], suffix_kv[0, 0], prefix_pool[0, 0], page_table[0])
    req_count = lax.psum(1, "req")
    projected = jnp.dot(
        gather_rows(attention, req_count).reshape(-1, attention.shape[-1]),
        out_weight,
        preferred_element_type=jnp.float32,
    )
    stream = (residual[0].astype(jnp.float32) + projected).astype(jnp.bfloat16)
    wide_local = stream.astype(jnp.float32)
    token_count, local_width = stream.shape
    with_gain = jnp.concatenate([stream, norm_gain.reshape(1, local_width)], axis=0)
    gathered = gather_rows(with_gain, req_count)
    full_stream = jnp.transpose(gathered[:, :token_count], (1, 0, 2)).reshape(token_count, -1)
    full_gain = gathered[:, token_count].reshape(-1)
    wide = full_stream.astype(jnp.float32)
    row_sumsq = jnp.sum(wide * wide, axis=1)
    inverse_rms = lax.rsqrt(row_sumsq / D + 1e-05)
    normed = (wide * inverse_rms[:, None] * full_gain.astype(jnp.float32)[None, :]).astype(
        jnp.bfloat16
    )
    gate_up_out = jnp.einsum(
        "nc,kcf->knf",
        normed,
        gate_up,
        preferred_element_type=jnp.float32,
    )
    hidden = (jax.nn.silu(gate_up_out[0]) * gate_up_out[1]).astype(jnp.bfloat16)
    partial_value = jnp.dot(hidden, down_weight, preferred_element_type=jnp.float32)
    blocks = jnp.transpose(
        partial_value.reshape(token_count, req_count, local_width), (1, 0, 2)
    )
    arrived = lax.all_to_all(blocks.astype(jnp.bfloat16), "req", 0, 0, tiled=False)
    summed = jnp.sum(arrived.astype(jnp.float32), axis=0)
    lengths = suffix_len[0]
    slot_index = jnp.arange(stream.shape[0], dtype=jnp.int32) % slot_count
    slot_live = (slot_index < jnp.repeat(lengths, slot_count)).astype(jnp.float32)
    result_rows = (wide_local + summed) * slot_live[:, None]
    return result_rows.astype(jnp.bfloat16)[None]


def solution(mesh):
    return jax.shard_map(
        body,
        mesh=mesh,
        in_specs=(
            P("grp", "req", None, None),
            P("grp", "req", None, None, None),
            P("grp", "req", None, None, None, None),
            P("req", None),
            P("grp", None),
            P("grp", None, "req"),
            P(None, "req"),
            P("req"),
            P(None, None, "req"),
            P("req", None),
        ),
        out_specs=P("grp", None, "req"),
        check_vma=False,
    )
```

```python
import jax
import jax.numpy as jnp
from jax import lax
from jax.sharding import PartitionSpec as P

D = 4096
HD = 128
QH = 16
KVH = 4
PAGE = 128


def heads_of(rows):
    row_count = rows.shape[0]
    return jnp.transpose(rows.reshape(row_count, KVH, QH // KVH, HD), (1, 2, 0, 3))


def attend(own_queries, own_suffix, own_pool, table_row):
    slot_count = own_queries.shape[0]
    member_count = lax.psum(1, "grp")
    member = lax.axis_index("grp")
    pool_pages = own_pool.shape[0]
    spread = jnp.broadcast_to(own_queries[None], (member_count,) + own_queries.shape)
    all_queries = lax.all_to_all(spread, "grp", 0, 0, tiled=False)
    query_heads = heads_of(all_queries.reshape(member_count * slot_count, -1))
    page_ids = member * pool_pages + jnp.arange(pool_pages, dtype=jnp.int32)
    page_used = jnp.any(page_ids[:, None] == table_row[None, :], axis=1)
    token_live = jnp.repeat(page_used, PAGE)
    key_rows = own_pool[:, 0].reshape(pool_pages * PAGE, KVH, HD)
    value_rows = own_pool[:, 1].reshape(pool_pages * PAGE, KVH, HD)
    scores = jnp.einsum(
        "jgsd,tjd->jgst", query_heads, key_rows, preferred_element_type=jnp.float32
    ) * HD ** (-0.5)
    scores = jnp.where(token_live, scores, -1e30)
    local_max = jnp.max(scores, axis=-1)
    weights = jnp.where(token_live, jnp.exp(scores - local_max[..., None]), 0.0)
    local_sum = jnp.sum(weights, axis=-1)
    weighted = jnp.einsum(
        "jgst,tjd->jgsd",
        weights.astype(jnp.bfloat16),
        value_rows,
        preferred_element_type=jnp.float32,
    )
    packed = jnp.concatenate([weighted, local_max[..., None], local_sum[..., None]], axis=-1)
    packed = packed.reshape(KVH, QH // KVH, member_count, slot_count, HD + 2)
    packed = jnp.transpose(packed, (2, 0, 1, 3, 4))
    parts = lax.all_to_all(packed, "grp", 0, 0, tiled=False)
    part_acc = parts[..., :HD]
    part_max = parts[..., HD]
    part_sum = parts[..., HD + 1]
    own_heads = heads_of(own_queries)
    suffix_keys = own_suffix[0].reshape(slot_count, KVH, HD)
    suffix_values = own_suffix[1].reshape(slot_count, KVH, HD)
    suffix_scores = jnp.einsum(
        "jgsd,tjd->jgst", own_heads, suffix_keys, preferred_element_type=jnp.float32
    ) * HD ** (-0.5)
    causal = jnp.arange(slot_count)[:, None] >= jnp.arange(slot_count)[None, :]
    suffix_scores = jnp.where(causal, suffix_scores, -1e30)
    merged_max = jnp.maximum(jnp.max(part_max, axis=0), jnp.max(suffix_scores, axis=-1))
    rescale = jnp.exp(part_max - merged_max[None])
    suffix_weights = jnp.where(causal, jnp.exp(suffix_scores - merged_max[..., None]), 0.0)
    total = jnp.sum(part_sum * rescale, axis=0) + jnp.sum(suffix_weights, axis=-1)
    accumulated = jnp.sum(part_acc * rescale[..., None], axis=0) + jnp.einsum(
        "jgst,tjd->jgsd",
        suffix_weights.astype(jnp.bfloat16),
        suffix_values,
        preferred_element_type=jnp.float32,
    )
    accumulated = accumulated / total[..., None]
    ordered = jnp.transpose(accumulated, (2, 0, 1, 3))
    return ordered.reshape(slot_count, QH * HD).astype(jnp.bfloat16)


def gather_rows(block, count):
    spread = jnp.broadcast_to(block[None], (count,) + block.shape)
    return lax.all_to_all(spread, "req", 0, 0, tiled=False)


def body(
    queries,
    suffix_kv,
    prefix_pool,
    page_table,
    suffix_len,
    residual,
    out_weight,
    norm_gain,
    gate_up,
    down_weight,
):
    slot_count = queries.shape[2]
    req_count = lax.psum(1, "req")
    full_gain = gather_rows(norm_gain, req_count).reshape(-1)
    attention = attend(queries[0, 0], suffix_kv[0, 0], prefix_pool[0, 0], page_table[0])
    projected = jnp.dot(
        gather_rows(attention, req_count).reshape(-1, attention.shape[-1]),
        out_weight,
        preferred_element_type=jnp.float32,
    )
    stream = (residual[0].astype(jnp.float32) + projected).astype(jnp.bfloat16)
    wide_local = stream.astype(jnp.float32)
    token_count, local_width = stream.shape
    gathered = gather_rows(stream, req_count)
    full_stream = jnp.transpose(gathered, (1, 0, 2)).reshape(token_count, -1)
    wide = full_stream.astype(jnp.float32)
    row_sumsq = jnp.sum(wide * wide, axis=1)
    inverse_rms = lax.rsqrt(row_sumsq / D + 1e-05)
    normed = (wide * inverse_rms[:, None] * full_gain.astype(jnp.float32)[None, :]).astype(
        jnp.bfloat16
    )
    gate_up_out = jnp.einsum(
        "nc,kcf->knf",
        normed,
        gate_up,
        preferred_element_type=jnp.float32,
    )
    hidden = (jax.nn.silu(gate_up_out[0]) * gate_up_out[1]).astype(jnp.bfloat16)
    partial_value = jnp.dot(hidden, down_weight, preferred_element_type=jnp.float32)
    blocks = jnp.transpose(
        partial_value.reshape(token_count, req_count, local_width), (1, 0, 2)
    )
    arrived = lax.all_to_all(blocks.astype(jnp.bfloat16), "req", 0, 0, tiled=False)
    summed = jnp.sum(arrived.astype(jnp.float32), axis=0)
    lengths = suffix_len[0]
    slot_index = jnp.arange(stream.shape[0], dtype=jnp.int32) % slot_count
    slot_live = (slot_index < jnp.repeat(lengths, slot_count)).astype(jnp.float32)
    result_rows = (wide_local + summed) * slot_live[:, None]
    return result_rows.astype(jnp.bfloat16)[None]


def solution(mesh):
    return jax.shard_map(
        body,
        mesh=mesh,
        in_specs=(
            P("grp", "req", None, None),
            P("grp", "req", None, None, None),
            P("grp", "req", None, None, None, None),
            P("req", None),
            P("grp", None),
            P("grp", None, "req"),
            P(None, "req"),
            P("req"),
            P(None, None, "req"),
            P("req", None),
        ),
        out_specs=P("grp", None, "req"),
        check_vma=False,
    )
```

```python
import jax
import jax.numpy as jnp
from jax import lax
from jax.sharding import PartitionSpec as P

D = 4096
HD = 128
QH = 16
KVH = 4
PAGE = 128


def heads_of(rows):
    row_count = rows.shape[0]
    return jnp.transpose(rows.reshape(row_count, KVH, QH // KVH, HD), (1, 2, 0, 3))


def attend(own_queries, own_suffix, own_pool, table_row):
    slot_count = own_queries.shape[0]
    member_count = lax.psum(1, "grp")
    member = lax.axis_index("grp")
    pool_pages = own_pool.shape[0]
    spread = jnp.broadcast_to(own_queries[None], (member_count,) + own_queries.shape)
    all_queries = lax.all_to_all(spread, "grp", 0, 0, tiled=False)
    query_heads = heads_of(all_queries.reshape(member_count * slot_count, -1))
    page_ids = member * pool_pages + jnp.arange(pool_pages, dtype=jnp.int32)
    page_used = jnp.any(page_ids[:, None] == table_row[None, :], axis=1)
    token_live = jnp.repeat(page_used, PAGE)
    key_rows = own_pool[:, 0].reshape(pool_pages * PAGE, KVH, HD)
    value_rows = own_pool[:, 1].reshape(pool_pages * PAGE, KVH, HD)
    scores = jnp.einsum(
        "jgsd,tjd->jgst", query_heads, key_rows, preferred_element_type=jnp.float32
    ) * HD ** (-0.5)
    scores = jnp.where(token_live, scores, -1e30)
    local_max = jnp.max(scores, axis=-1)
    weights = jnp.where(token_live, jnp.exp(scores - local_max[..., None]), 0.0)
    local_sum = jnp.sum(weights, axis=-1)
    weighted = jnp.einsum(
        "jgst,tjd->jgsd",
        weights.astype(jnp.bfloat16),
        value_rows,
        preferred_element_type=jnp.float32,
    )
    packed = jnp.concatenate([weighted, local_max[..., None], local_sum[..., None]], axis=-1)
    packed = packed.reshape(KVH, QH // KVH, member_count, slot_count, HD + 2)
    packed = jnp.transpose(packed, (2, 0, 1, 3, 4))
    parts = lax.all_to_all(packed, "grp", 0, 0, tiled=False)
    part_acc = parts[..., :HD]
    part_max = parts[..., HD]
    part_sum = parts[..., HD + 1]
    own_heads = heads_of(own_queries)
    suffix_keys = own_suffix[0].reshape(slot_count, KVH, HD)
    suffix_values = own_suffix[1].reshape(slot_count, KVH, HD)
    suffix_scores = jnp.einsum(
        "jgsd,tjd->jgst", own_heads, suffix_keys, preferred_element_type=jnp.float32
    ) * HD ** (-0.5)
    causal = jnp.arange(slot_count)[:, None] >= jnp.arange(slot_count)[None, :]
    suffix_scores = jnp.where(causal, suffix_scores, -1e30)
    merged_max = jnp.maximum(jnp.max(part_max, axis=0), jnp.max(suffix_scores, axis=-1))
    rescale = jnp.exp(part_max - merged_max[None])
    suffix_weights = jnp.where(causal, jnp.exp(suffix_scores - merged_max[..., None]), 0.0)
    total = jnp.sum(part_sum * rescale, axis=0) + jnp.sum(suffix_weights, axis=-1)
    accumulated = jnp.sum(part_acc * rescale[..., None], axis=0) + jnp.einsum(
        "jgst,tjd->jgsd",
        suffix_weights.astype(jnp.bfloat16),
        suffix_values,
        preferred_element_type=jnp.float32,
    )
    accumulated = accumulated / total[..., None]
    ordered = jnp.transpose(accumulated, (2, 0, 1, 3))
    return ordered.reshape(slot_count, QH * HD).astype(jnp.bfloat16)


def gather_rows(block, count):
    spread = jnp.broadcast_to(block[None], (count,) + block.shape)
    return lax.all_to_all(spread, "req", 0, 0, tiled=False)


def body(
    queries,
    suffix_kv,
    prefix_pool,
    page_table,
    suffix_len,
    residual,
    out_weight,
    norm_gain,
    gate_up,
    down_weight,
):
    slot_count = queries.shape[2]
    req_count = lax.psum(1, "req")
    attention = attend(queries[0, 0], suffix_kv[0, 0], prefix_pool[0, 0], page_table[0])
    gain_cols = norm_gain.shape[0] // slot_count
    gain_block = jnp.pad(norm_gain.reshape(slot_count, gain_cols), ((0, 0), (0, HD - gain_cols)))
    gathered_rows = gather_rows(jnp.concatenate([attention, gain_block], axis=1), req_count)
    full_gain = gathered_rows[:, :, QH * HD : QH * HD + gain_cols].reshape(-1)
    projected = jnp.dot(
        gathered_rows[:, :, : QH * HD].reshape(-1, QH * HD),
        out_weight,
        preferred_element_type=jnp.float32,
    )
    stream = (residual[0].astype(jnp.float32) + projected).astype(jnp.bfloat16)
    wide_local = stream.astype(jnp.float32)
    token_count, local_width = stream.shape
    gathered = gather_rows(stream, req_count)
    full_stream = jnp.transpose(gathered, (1, 0, 2)).reshape(token_count, -1)
    wide = full_stream.astype(jnp.float32)
    row_sumsq = jnp.sum(wide * wide, axis=1)
    inverse_rms = lax.rsqrt(row_sumsq / D + 1e-05)
    normed = (wide * inverse_rms[:, None] * full_gain.astype(jnp.float32)[None, :]).astype(
        jnp.bfloat16
    )
    gate_up_out = jnp.einsum(
        "nc,kcf->knf",
        normed,
        gate_up,
        preferred_element_type=jnp.float32,
    )
    hidden = (jax.nn.silu(gate_up_out[0]) * gate_up_out[1]).astype(jnp.bfloat16)
    partial_value = jnp.dot(hidden, down_weight, preferred_element_type=jnp.float32)
    blocks = jnp.transpose(
        partial_value.reshape(token_count, req_count, local_width), (1, 0, 2)
    )
    arrived = lax.all_to_all(blocks.astype(jnp.bfloat16), "req", 0, 0, tiled=False)
    summed = jnp.sum(arrived.astype(jnp.float32), axis=0)
    lengths = suffix_len[0]
    slot_index = jnp.arange(stream.shape[0], dtype=jnp.int32) % slot_count
    slot_live = (slot_index < jnp.repeat(lengths, slot_count)).astype(jnp.float32)
    result_rows = (wide_local + summed) * slot_live[:, None]
    return result_rows.astype(jnp.bfloat16)[None]


def solution(mesh):
    return jax.shard_map(
        body,
        mesh=mesh,
        in_specs=(
            P("grp", "req", None, None),
            P("grp", "req", None, None, None),
            P("grp", "req", None, None, None, None),
            P("req", None),
            P("grp", None),
            P("grp", None, "req"),
            P(None, "req"),
            P("req"),
            P(None, None, "req"),
            P("req", None),
        ),
        out_specs=P("grp", None, "req"),
        check_vma=False,
    )
```

```python
import jax
import jax.numpy as jnp
from jax import lax
from jax.sharding import PartitionSpec as P

D = 4096
HD = 128
QH = 16
KVH = 4
PAGE = 128


def heads_of(rows):
    row_count = rows.shape[0]
    return jnp.transpose(rows.reshape(row_count, KVH, QH // KVH, HD), (1, 2, 0, 3))


def attend(own_queries, own_suffix, own_pool, table_row):
    slot_count = own_queries.shape[0]
    member_count = lax.psum(1, "grp")
    member = lax.axis_index("grp")
    pool_pages = own_pool.shape[0]
    spread = jnp.broadcast_to(own_queries[None], (member_count,) + own_queries.shape)
    all_queries = lax.all_to_all(spread, "grp", 0, 0, tiled=False)
    query_heads = heads_of(all_queries.reshape(member_count * slot_count, -1))
    page_ids = member * pool_pages + jnp.arange(pool_pages, dtype=jnp.int32)
    page_used = jnp.any(page_ids[:, None] == table_row[None, :], axis=1)
    token_live = jnp.repeat(page_used, PAGE)
    key_rows = own_pool[:, 0].reshape(pool_pages * PAGE, KVH, HD)
    value_rows = own_pool[:, 1].reshape(pool_pages * PAGE, KVH, HD)
    scores = jnp.einsum(
        "jgsd,tjd->jgst", query_heads, key_rows, preferred_element_type=jnp.float32
    ) * HD ** (-0.5)
    scores = jnp.where(token_live, scores, -1e30)
    local_max = jnp.max(scores, axis=-1)
    weights = jnp.where(token_live, jnp.exp(scores - local_max[..., None]), 0.0)
    local_sum = jnp.sum(weights, axis=-1)
    weighted = jnp.einsum(
        "jgst,tjd->jgsd",
        weights.astype(jnp.bfloat16),
        value_rows,
        preferred_element_type=jnp.float32,
    )
    packed = jnp.concatenate([weighted, local_max[..., None], local_sum[..., None]], axis=-1)
    packed = packed.reshape(KVH, QH // KVH, member_count, slot_count, HD + 2)
    packed = jnp.transpose(packed, (2, 0, 1, 3, 4))
    parts = lax.all_to_all(packed, "grp", 0, 0, tiled=False)
    part_acc = parts[..., :HD]
    part_max = parts[..., HD]
    part_sum = parts[..., HD + 1]
    own_heads = heads_of(own_queries)
    suffix_keys = own_suffix[0].reshape(slot_count, KVH, HD)
    suffix_values = own_suffix[1].reshape(slot_count, KVH, HD)
    suffix_scores = jnp.einsum(
        "jgsd,tjd->jgst", own_heads, suffix_keys, preferred_element_type=jnp.float32
    ) * HD ** (-0.5)
    causal = jnp.arange(slot_count)[:, None] >= jnp.arange(slot_count)[None, :]
    suffix_scores = jnp.where(causal, suffix_scores, -1e30)
    merged_max = jnp.maximum(jnp.max(part_max, axis=0), jnp.max(suffix_scores, axis=-1))
    rescale = jnp.exp(part_max - merged_max[None])
    suffix_weights = jnp.where(causal, jnp.exp(suffix_scores - merged_max[..., None]), 0.0)
    total = jnp.sum(part_sum * rescale, axis=0) + jnp.sum(suffix_weights, axis=-1)
    accumulated = jnp.sum(part_acc * rescale[..., None], axis=0) + jnp.einsum(
        "jgst,tjd->jgsd",
        suffix_weights.astype(jnp.bfloat16),
        suffix_values,
        preferred_element_type=jnp.float32,
    )
    accumulated = accumulated / total[..., None]
    ordered = jnp.transpose(accumulated, (2, 0, 1, 3))
    return ordered.reshape(slot_count, QH * HD).astype(jnp.bfloat16)


def gather_rows(block, count):
    spread = jnp.broadcast_to(block[None], (count,) + block.shape)
    return lax.all_to_all(spread, "req", 0, 0, tiled=False)


def body(
    queries,
    suffix_kv,
    prefix_pool,
    page_table,
    suffix_len,
    residual,
    out_weight,
    norm_gain,
    gate_up,
    down_weight,
):
    slot_count = queries.shape[2]
    req_count = lax.psum(1, "req")
    attention = attend(queries[0, 0], suffix_kv[0, 0], prefix_pool[0, 0], page_table[0])
    gain_cols = norm_gain.shape[0] // slot_count
    gain_block = jnp.pad(norm_gain.reshape(slot_count, gain_cols), ((0, 0), (0, HD - gain_cols)))
    gathered_rows = gather_rows(jnp.concatenate([attention, gain_block], axis=1), req_count)
    full_gain = gathered_rows[:, :, QH * HD : QH * HD + gain_cols].reshape(-1)
    token_count = residual.shape[1]
    live_count = token_count // 2
    lengths = suffix_len[0]
    slot_index = jnp.arange(token_count, dtype=jnp.int32) % slot_count
    slot_live = slot_index < jnp.repeat(lengths, slot_count)
    live_rank = jnp.cumsum(slot_live.astype(jnp.int32)) - 1
    live_rows = jnp.zeros((live_count,), jnp.int32).at[
        jnp.where(slot_live, live_rank, live_count)
    ].set(jnp.arange(token_count, dtype=jnp.int32), mode="drop")
    all_rows = gathered_rows[:, :, : QH * HD].reshape(-1, QH * HD)
    projected = jnp.dot(
        jnp.take(all_rows, live_rows, axis=0),
        out_weight,
        preferred_element_type=jnp.float32,
    )
    own_residual = jnp.take(residual[0], live_rows, axis=0)
    stream = (own_residual.astype(jnp.float32) + projected).astype(jnp.bfloat16)
    wide_local = stream.astype(jnp.float32)
    local_width = stream.shape[1]
    gathered = gather_rows(stream, req_count)
    full_stream = jnp.transpose(gathered, (1, 0, 2)).reshape(live_count, -1)
    wide = full_stream.astype(jnp.float32)
    row_sumsq = jnp.sum(wide * wide, axis=1)
    inverse_rms = lax.rsqrt(row_sumsq / D + 1e-05)
    normed = (wide * inverse_rms[:, None] * full_gain.astype(jnp.float32)[None, :]).astype(
        jnp.bfloat16
    )
    gate_up_out = jnp.einsum(
        "nc,kcf->knf",
        normed,
        gate_up,
        preferred_element_type=jnp.float32,
    )
    hidden = (jax.nn.silu(gate_up_out[0]) * gate_up_out[1]).astype(jnp.bfloat16)
    partial_value = jnp.dot(hidden, down_weight, preferred_element_type=jnp.float32)
    blocks = jnp.transpose(
        partial_value.reshape(live_count, req_count, local_width), (1, 0, 2)
    )
    arrived = lax.all_to_all(blocks.astype(jnp.bfloat16), "req", 0, 0, tiled=False)
    summed = jnp.sum(arrived.astype(jnp.float32), axis=0)
    live_values = (wide_local + summed).astype(jnp.bfloat16)
    result_rows = jnp.zeros((token_count, local_width), jnp.bfloat16).at[live_rows].set(live_values)
    return result_rows.astype(jnp.bfloat16)[None]


def solution(mesh):
    return jax.shard_map(
        body,
        mesh=mesh,
        in_specs=(
            P("grp", "req", None, None),
            P("grp", "req", None, None, None),
            P("grp", "req", None, None, None, None),
            P("req", None),
            P("grp", None),
            P("grp", None, "req"),
            P(None, "req"),
            P("req"),
            P(None, None, "req"),
            P("req", None),
        ),
        out_specs=P("grp", None, "req"),
        check_vma=False,
    )
```

```python
import jax
import jax.numpy as jnp
from jax import lax
from jax.sharding import PartitionSpec as P

D = 4096
HD = 128
QH = 16
KVH = 4
PAGE = 128


def heads_of(rows):
    row_count = rows.shape[0]
    return jnp.transpose(rows.reshape(row_count, KVH, QH // KVH, HD), (1, 2, 0, 3))


def attend(own_queries, own_suffix, own_pool, table_row):
    slot_count = own_queries.shape[0]
    member_count = lax.psum(1, "grp")
    member = lax.axis_index("grp")
    pool_pages = own_pool.shape[0]
    spread = jnp.broadcast_to(own_queries[None], (member_count,) + own_queries.shape)
    all_queries = lax.all_to_all(spread, "grp", 0, 0, tiled=False)
    query_heads = heads_of(all_queries.reshape(member_count * slot_count, -1))
    page_ids = member * pool_pages + jnp.arange(pool_pages, dtype=jnp.int32)
    page_used = jnp.any(page_ids[:, None] == table_row[None, :], axis=1)
    token_live = jnp.repeat(page_used, PAGE)
    key_rows = own_pool[:, 0].reshape(pool_pages * PAGE, KVH, HD)
    value_rows = own_pool[:, 1].reshape(pool_pages * PAGE, KVH, HD)
    scores = jnp.einsum(
        "jgsd,tjd->jgst", query_heads, key_rows, preferred_element_type=jnp.float32
    ) * HD ** (-0.5)
    scores = jnp.where(token_live, scores, -1e30)
    local_max = jnp.max(scores, axis=-1)
    weights = jnp.where(token_live, jnp.exp(scores - local_max[..., None]), 0.0)
    local_sum = jnp.sum(weights, axis=-1)
    weighted = jnp.einsum(
        "jgst,tjd->jgsd",
        weights.astype(jnp.bfloat16),
        value_rows,
        preferred_element_type=jnp.float32,
    )
    packed = jnp.concatenate([weighted, local_max[..., None], local_sum[..., None]], axis=-1)
    packed = packed.reshape(KVH, QH // KVH, member_count, slot_count, HD + 2)
    packed = jnp.transpose(packed, (2, 0, 1, 3, 4))
    parts = lax.all_to_all(packed, "grp", 0, 0, tiled=False)
    part_acc = parts[..., :HD]
    part_max = parts[..., HD]
    part_sum = parts[..., HD + 1]
    own_heads = heads_of(own_queries)
    suffix_keys = own_suffix[0].reshape(slot_count, KVH, HD)
    suffix_values = own_suffix[1].reshape(slot_count, KVH, HD)
    suffix_scores = jnp.einsum(
        "jgsd,tjd->jgst", own_heads, suffix_keys, preferred_element_type=jnp.float32
    ) * HD ** (-0.5)
    causal = jnp.arange(slot_count)[:, None] >= jnp.arange(slot_count)[None, :]
    suffix_scores = jnp.where(causal, suffix_scores, -1e30)
    merged_max = jnp.maximum(jnp.max(part_max, axis=0), jnp.max(suffix_scores, axis=-1))
    rescale = jnp.exp(part_max - merged_max[None])
    suffix_weights = jnp.where(causal, jnp.exp(suffix_scores - merged_max[..., None]), 0.0)
    total = jnp.sum(part_sum * rescale, axis=0) + jnp.sum(suffix_weights, axis=-1)
    accumulated = jnp.sum(part_acc * rescale[..., None], axis=0) + jnp.einsum(
        "jgst,tjd->jgsd",
        suffix_weights.astype(jnp.bfloat16),
        suffix_values,
        preferred_element_type=jnp.float32,
    )
    accumulated = accumulated / total[..., None]
    ordered = jnp.transpose(accumulated, (2, 0, 1, 3))
    return ordered.reshape(slot_count, QH * HD).astype(jnp.bfloat16)


def gather_rows(block, count):
    spread = jnp.broadcast_to(block[None], (count,) + block.shape)
    return lax.all_to_all(spread, "req", 0, 0, tiled=False)


def body(
    queries,
    suffix_kv,
    prefix_pool,
    page_table,
    suffix_len,
    residual,
    out_weight,
    norm_gain,
    gate_up,
    down_weight,
):
    slot_count = queries.shape[2]
    req_count = lax.psum(1, "req")
    attention = attend(queries[0, 0], suffix_kv[0, 0], prefix_pool[0, 0], page_table[0])
    gain_cols = norm_gain.shape[0] // slot_count
    gain_block = jnp.pad(norm_gain.reshape(slot_count, gain_cols), ((0, 0), (0, HD - gain_cols)))
    gathered_rows = gather_rows(jnp.concatenate([attention, gain_block], axis=1), req_count)
    full_gain = gathered_rows[:, :, QH * HD : QH * HD + gain_cols].reshape(-1)
    token_count = residual.shape[1]
    live_count = token_count // 2
    lengths = suffix_len[0]
    slot_index = jnp.arange(token_count, dtype=jnp.int32) % slot_count
    slot_live = slot_index < jnp.repeat(lengths, slot_count)
    live_rank = jnp.cumsum(slot_live.astype(jnp.int32)) - 1
    live_rows = jnp.zeros((live_count,), jnp.int32).at[
        jnp.where(slot_live, live_rank, live_count)
    ].set(jnp.arange(token_count, dtype=jnp.int32), mode="drop")
    live_heads = gathered_rows[live_rows // slot_count, live_rows % slot_count, : QH * HD]
    projected = jnp.dot(
        live_heads,
        out_weight,
        preferred_element_type=jnp.float32,
    )
    own_residual = jnp.take(residual[0], live_rows, axis=0)
    stream = (own_residual.astype(jnp.float32) + projected).astype(jnp.bfloat16)
    wide_local = stream.astype(jnp.float32)
    local_width = stream.shape[1]
    gathered = gather_rows(stream, req_count)
    full_stream = jnp.transpose(gathered, (1, 0, 2)).reshape(live_count, -1)
    wide = full_stream.astype(jnp.float32)
    row_sumsq = jnp.sum(wide * wide, axis=1)
    inverse_rms = lax.rsqrt(row_sumsq / D + 1e-05)
    normed = (wide * inverse_rms[:, None] * full_gain.astype(jnp.float32)[None, :]).astype(
        jnp.bfloat16
    )
    gate_up_out = jnp.einsum(
        "nc,kcf->knf",
        normed,
        gate_up,
        preferred_element_type=jnp.float32,
    )
    hidden = (jax.nn.silu(gate_up_out[0]) * gate_up_out[1]).astype(jnp.bfloat16)
    partial_value = jnp.dot(hidden, down_weight, preferred_element_type=jnp.float32)
    blocks = jnp.transpose(
        partial_value.reshape(live_count, req_count, local_width), (1, 0, 2)
    )
    arrived = lax.all_to_all(blocks.astype(jnp.bfloat16), "req", 0, 0, tiled=False)
    summed = jnp.sum(arrived.astype(jnp.float32), axis=0)
    live_values = (wide_local + summed).astype(jnp.bfloat16)
    result_rows = jnp.zeros((token_count, local_width), jnp.bfloat16).at[live_rows].set(live_values)
    return result_rows.astype(jnp.bfloat16)[None]


def solution(mesh):
    return jax.shard_map(
        body,
        mesh=mesh,
        in_specs=(
            P("grp", "req", None, None),
            P("grp", "req", None, None, None),
            P("grp", "req", None, None, None, None),
            P("req", None),
            P("grp", None),
            P("grp", None, "req"),
            P(None, "req"),
            P("req"),
            P(None, None, "req"),
            P("req", None),
        ),
        out_specs=P("grp", None, "req"),
        check_vma=False,
    )
```

```python
import jax
import jax.numpy as jnp
from jax import lax
from jax.sharding import PartitionSpec as P

D = 4096
HD = 128
QH = 16
KVH = 4
PAGE = 128


def heads_of(rows):
    row_count = rows.shape[0]
    return jnp.transpose(rows.reshape(row_count, KVH, QH // KVH, HD), (1, 2, 0, 3))


def attend(own_queries, own_suffix, own_pool, table_row):
    slot_count = own_queries.shape[0]
    member_count = lax.psum(1, "grp")
    member = lax.axis_index("grp")
    pool_pages = own_pool.shape[0]
    spread = jnp.broadcast_to(own_queries[None], (member_count,) + own_queries.shape)
    all_queries = lax.all_to_all(spread, "grp", 0, 0, tiled=False)
    query_heads = heads_of(all_queries.reshape(member_count * slot_count, -1))
    page_ids = member * pool_pages + jnp.arange(pool_pages, dtype=jnp.int32)
    page_used = jnp.any(page_ids[:, None] == table_row[None, :], axis=1)
    token_live = jnp.repeat(page_used, PAGE)
    key_rows = own_pool[:, 0].reshape(pool_pages * PAGE, KVH, HD)
    value_rows = own_pool[:, 1].reshape(pool_pages * PAGE, KVH, HD)
    scores = jnp.einsum(
        "jgsd,tjd->jgst", query_heads, key_rows, preferred_element_type=jnp.float32
    ) * HD ** (-0.5)
    scores = jnp.where(token_live, scores, -1e30)
    local_max = jnp.max(scores, axis=-1)
    weights = jnp.where(token_live, jnp.exp(scores - local_max[..., None]), 0.0)
    local_sum = jnp.sum(weights, axis=-1)
    weighted = jnp.einsum(
        "jgst,tjd->jgsd",
        weights.astype(jnp.bfloat16),
        value_rows,
        preferred_element_type=jnp.float32,
    )
    packed = jnp.concatenate([weighted, local_max[..., None], local_sum[..., None]], axis=-1)
    packed = packed.reshape(KVH, QH // KVH, member_count, slot_count, HD + 2)
    packed = jnp.transpose(packed, (2, 0, 1, 3, 4))
    parts = lax.all_to_all(packed, "grp", 0, 0, tiled=False)
    part_acc = parts[..., :HD]
    part_max = parts[..., HD]
    part_sum = parts[..., HD + 1]
    own_heads = heads_of(own_queries)
    suffix_keys = own_suffix[0].reshape(slot_count, KVH, HD)
    suffix_values = own_suffix[1].reshape(slot_count, KVH, HD)
    suffix_scores = jnp.einsum(
        "jgsd,tjd->jgst", own_heads, suffix_keys, preferred_element_type=jnp.float32
    ) * HD ** (-0.5)
    causal = jnp.arange(slot_count)[:, None] >= jnp.arange(slot_count)[None, :]
    suffix_scores = jnp.where(causal, suffix_scores, -1e30)
    merged_max = jnp.maximum(jnp.max(part_max, axis=0), jnp.max(suffix_scores, axis=-1))
    rescale = jnp.exp(part_max - merged_max[None])
    suffix_weights = jnp.where(causal, jnp.exp(suffix_scores - merged_max[..., None]), 0.0)
    total = jnp.sum(part_sum * rescale, axis=0) + jnp.sum(suffix_weights, axis=-1)
    accumulated = jnp.sum(part_acc * rescale[..., None], axis=0) + jnp.einsum(
        "jgst,tjd->jgsd",
        suffix_weights.astype(jnp.bfloat16),
        suffix_values,
        preferred_element_type=jnp.float32,
    )
    accumulated = accumulated / total[..., None]
    ordered = jnp.transpose(accumulated, (2, 0, 1, 3))
    return ordered.reshape(slot_count, QH * HD).astype(jnp.bfloat16)


def gather_rows(block, count):
    spread = jnp.broadcast_to(block[None], (count,) + block.shape)
    return lax.all_to_all(spread, "req", 0, 0, tiled=False)


def body(
    queries,
    suffix_kv,
    prefix_pool,
    page_table,
    suffix_len,
    residual,
    out_weight,
    norm_gain,
    gate_up,
    down_weight,
):
    slot_count = queries.shape[2]
    req_count = lax.psum(1, "req")
    attention = attend(queries[0, 0], suffix_kv[0, 0], prefix_pool[0, 0], page_table[0])
    gain_cols = norm_gain.shape[0] // slot_count
    gain_block = jnp.pad(norm_gain.reshape(slot_count, gain_cols), ((0, 0), (0, HD - gain_cols)))
    gathered_rows = gather_rows(jnp.concatenate([attention, gain_block], axis=1), req_count)
    full_gain = gathered_rows[:, :, QH * HD : QH * HD + gain_cols].reshape(-1)
    token_count = residual.shape[1]
    live_count = token_count // 2
    lengths = suffix_len[0]
    slot_index = jnp.arange(token_count, dtype=jnp.int32) % slot_count
    slot_live = slot_index < jnp.repeat(lengths, slot_count)
    live_rank = jnp.cumsum(slot_live.astype(jnp.int32)) - 1
    live_rows = jnp.zeros((live_count,), jnp.int32).at[
        jnp.where(slot_live, live_rank, live_count)
    ].set(jnp.arange(token_count, dtype=jnp.int32), mode="drop")
    all_rows = gathered_rows.reshape(token_count, -1)
    projected = jnp.dot(
        jnp.take(all_rows, live_rows, axis=0)[:, : QH * HD],
        out_weight,
        preferred_element_type=jnp.float32,
    )
    own_residual = jnp.take(residual[0], live_rows, axis=0)
    stream = (own_residual.astype(jnp.float32) + projected).astype(jnp.bfloat16)
    wide_local = stream.astype(jnp.float32)
    local_width = stream.shape[1]
    gathered = gather_rows(stream, req_count)
    full_stream = jnp.transpose(gathered, (1, 0, 2)).reshape(live_count, -1)
    wide = full_stream.astype(jnp.float32)
    row_sumsq = jnp.sum(wide * wide, axis=1)
    inverse_rms = lax.rsqrt(row_sumsq / D + 1e-05)
    normed = (wide * inverse_rms[:, None] * full_gain.astype(jnp.float32)[None, :]).astype(
        jnp.bfloat16
    )
    gate_up_out = jnp.einsum(
        "nc,kcf->knf",
        normed,
        gate_up,
        preferred_element_type=jnp.float32,
    )
    hidden = (jax.nn.silu(gate_up_out[0]) * gate_up_out[1]).astype(jnp.bfloat16)
    partial_value = jnp.dot(hidden, down_weight, preferred_element_type=jnp.float32)
    blocks = jnp.transpose(
        partial_value.reshape(live_count, req_count, local_width), (1, 0, 2)
    )
    arrived = lax.all_to_all(blocks.astype(jnp.bfloat16), "req", 0, 0, tiled=False)
    summed = jnp.sum(arrived.astype(jnp.float32), axis=0)
    live_values = (wide_local + summed).astype(jnp.bfloat16)
    result_rows = jnp.zeros((token_count, local_width), jnp.bfloat16).at[live_rows].set(live_values)
    return result_rows.astype(jnp.bfloat16)[None]


def solution(mesh):
    return jax.shard_map(
        body,
        mesh=mesh,
        in_specs=(
            P("grp", "req", None, None),
            P("grp", "req", None, None, None),
            P("grp", "req", None, None, None, None),
            P("req", None),
            P("grp", None),
            P("grp", None, "req"),
            P(None, "req"),
            P("req"),
            P(None, None, "req"),
            P("req", None),
        ),
        out_specs=P("grp", None, "req"),
        check_vma=False,
    )
```

```python
import jax
import jax.numpy as jnp
from jax import lax
from jax.sharding import PartitionSpec as P

D = 4096
HD = 128
QH = 16
KVH = 4
PAGE = 128


def heads_of(rows):
    row_count = rows.shape[0]
    return jnp.transpose(rows.reshape(row_count, KVH, QH // KVH, HD), (1, 2, 0, 3))


def attend(own_queries, own_suffix, own_pool, table_row):
    slot_count = own_queries.shape[0]
    member_count = lax.psum(1, "grp")
    member = lax.axis_index("grp")
    pool_pages = own_pool.shape[0]
    spread = jnp.broadcast_to(own_queries[None], (member_count,) + own_queries.shape)
    all_queries = lax.all_to_all(spread, "grp", 0, 0, tiled=False)
    query_heads = heads_of(all_queries.reshape(member_count * slot_count, -1))
    page_ids = member * pool_pages + jnp.arange(pool_pages, dtype=jnp.int32)
    page_used = jnp.any(page_ids[:, None] == table_row[None, :], axis=1)
    token_live = jnp.repeat(page_used, PAGE)
    key_rows = own_pool[:, 0].reshape(pool_pages * PAGE, KVH, HD)
    value_rows = own_pool[:, 1].reshape(pool_pages * PAGE, KVH, HD)
    scores = jnp.einsum(
        "jgsd,tjd->jgst", query_heads, key_rows, preferred_element_type=jnp.float32
    ) * HD ** (-0.5)
    scores = jnp.where(token_live, scores, -1e30)
    local_max = jnp.max(scores, axis=-1)
    weights = jnp.where(token_live, jnp.exp(scores - local_max[..., None]), 0.0)
    local_sum = jnp.sum(weights, axis=-1)
    weighted = jnp.einsum(
        "jgst,tjd->jgsd",
        weights.astype(jnp.bfloat16),
        value_rows,
        preferred_element_type=jnp.float32,
    )
    def by_member(part):
        split = part.reshape(KVH, QH // KVH, member_count, slot_count, -1)
        return jnp.transpose(split, (2, 0, 1, 3, 4)).reshape(member_count, QH * slot_count, -1)

    stats = jnp.concatenate([by_member(local_max[..., None]), by_member(local_sum[..., None])], axis=1)
    packed = jnp.concatenate([by_member(weighted), jnp.transpose(stats, (0, 2, 1))], axis=1)
    parts = lax.all_to_all(packed, "grp", 0, 0, tiled=False)
    head_shape = (member_count, KVH, QH // KVH, slot_count)
    part_acc = parts[:, : QH * slot_count].reshape(head_shape + (HD,))
    part_max = parts[:, QH * slot_count, : QH * slot_count].reshape(head_shape)
    part_sum = parts[:, QH * slot_count, QH * slot_count :].reshape(head_shape)
    own_heads = heads_of(own_queries)
    suffix_keys = own_suffix[0].reshape(slot_count, KVH, HD)
    suffix_values = own_suffix[1].reshape(slot_count, KVH, HD)
    suffix_scores = jnp.einsum(
        "jgsd,tjd->jgst", own_heads, suffix_keys, preferred_element_type=jnp.float32
    ) * HD ** (-0.5)
    causal = jnp.arange(slot_count)[:, None] >= jnp.arange(slot_count)[None, :]
    suffix_scores = jnp.where(causal, suffix_scores, -1e30)
    merged_max = jnp.maximum(jnp.max(part_max, axis=0), jnp.max(suffix_scores, axis=-1))
    rescale = jnp.exp(part_max - merged_max[None])
    suffix_weights = jnp.where(causal, jnp.exp(suffix_scores - merged_max[..., None]), 0.0)
    total = jnp.sum(part_sum * rescale, axis=0) + jnp.sum(suffix_weights, axis=-1)
    accumulated = jnp.sum(part_acc * rescale[..., None], axis=0) + jnp.einsum(
        "jgst,tjd->jgsd",
        suffix_weights.astype(jnp.bfloat16),
        suffix_values,
        preferred_element_type=jnp.float32,
    )
    accumulated = accumulated / total[..., None]
    ordered = jnp.transpose(accumulated, (2, 0, 1, 3))
    return ordered.reshape(slot_count, QH * HD).astype(jnp.bfloat16)


def gather_rows(block, count):
    spread = jnp.broadcast_to(block[None], (count,) + block.shape)
    return lax.all_to_all(spread, "req", 0, 0, tiled=False)


def body(
    queries,
    suffix_kv,
    prefix_pool,
    page_table,
    suffix_len,
    residual,
    out_weight,
    norm_gain,
    gate_up,
    down_weight,
):
    slot_count = queries.shape[2]
    req_count = lax.psum(1, "req")
    attention = attend(queries[0, 0], suffix_kv[0, 0], prefix_pool[0, 0], page_table[0])
    gain_cols = norm_gain.shape[0] // slot_count
    gain_block = jnp.pad(norm_gain.reshape(slot_count, gain_cols), ((0, 0), (0, HD - gain_cols)))
    gathered_rows = gather_rows(jnp.concatenate([attention, gain_block], axis=1), req_count)
    full_gain = gathered_rows[:, :, QH * HD : QH * HD + gain_cols].reshape(-1)
    token_count = residual.shape[1]
    live_count = token_count // 2
    lengths = suffix_len[0]
    slot_index = jnp.arange(token_count, dtype=jnp.int32) % slot_count
    slot_live = slot_index < jnp.repeat(lengths, slot_count)
    live_rank = jnp.cumsum(slot_live.astype(jnp.int32)) - 1
    live_rows = jnp.zeros((live_count,), jnp.int32).at[
        jnp.where(slot_live, live_rank, live_count)
    ].set(jnp.arange(token_count, dtype=jnp.int32), mode="drop")
    all_rows = gathered_rows.reshape(token_count, -1)
    projected = jnp.dot(
        jnp.take(all_rows, live_rows, axis=0)[:, : QH * HD],
        out_weight,
        preferred_element_type=jnp.float32,
    )
    own_residual = jnp.take(residual[0], live_rows, axis=0)
    stream = (own_residual.astype(jnp.float32) + projected).astype(jnp.bfloat16)
    wide_local = stream.astype(jnp.float32)
    local_width = stream.shape[1]
    gathered = gather_rows(stream, req_count)
    full_stream = jnp.transpose(gathered, (1, 0, 2)).reshape(live_count, -1)
    wide = full_stream.astype(jnp.float32)
    row_sumsq = jnp.sum(wide * wide, axis=1)
    inverse_rms = lax.rsqrt(row_sumsq / D + 1e-05)
    normed = (wide * inverse_rms[:, None] * full_gain.astype(jnp.float32)[None, :]).astype(
        jnp.bfloat16
    )
    gate_up_out = jnp.einsum(
        "nc,kcf->knf",
        normed,
        gate_up,
        preferred_element_type=jnp.float32,
    )
    hidden = (jax.nn.silu(gate_up_out[0]) * gate_up_out[1]).astype(jnp.bfloat16)
    partial_value = jnp.dot(hidden, down_weight, preferred_element_type=jnp.float32)
    blocks = jnp.transpose(
        partial_value.reshape(live_count, req_count, local_width), (1, 0, 2)
    )
    arrived = lax.all_to_all(blocks.astype(jnp.bfloat16), "req", 0, 0, tiled=False)
    summed = jnp.sum(arrived.astype(jnp.float32), axis=0)
    live_values = (wide_local + summed).astype(jnp.bfloat16)
    result_rows = jnp.zeros((token_count, local_width), jnp.bfloat16).at[live_rows].set(live_values)
    return result_rows.astype(jnp.bfloat16)[None]


def solution(mesh):
    return jax.shard_map(
        body,
        mesh=mesh,
        in_specs=(
            P("grp", "req", None, None),
            P("grp", "req", None, None, None),
            P("grp", "req", None, None, None, None),
            P("req", None),
            P("grp", None),
            P("grp", None, "req"),
            P(None, "req"),
            P("req"),
            P(None, None, "req"),
            P("req", None),
        ),
        out_specs=P("grp", None, "req"),
        check_vma=False,
    )
```
